512 devices in a mesh: section: 64 (over z, y_hi, core), expert: 8 (over x, y_lo).
Axes of the slice: x: 4, y: 4 (y_hi: 2, y_lo: 2; y = y_hi * 2 + y_lo), z: 16, core: 2. Of those that a mesh axis runs over, the one named last changes fastest.
Arguments:
- tokens: bfloat16 [65536, 2048], P(('section', 'expert')), may hold values from -6 to 6
- routes: int32 [2, 65536, 2], P(None, ('section', 'expert')), may hold values from 0 to 7, all different within a row; in each aligned block of 128 rows (0 to 127, 128 to 255, ..., all dimensions but the last counted through in order) at most 36 rows name the same one
- combine: float32 [2, 65536, 2], P(None, ('section', 'expert')), may hold values from 0.25 to 4
- up_weight: bfloat16 [64, 8, 2048, 512], P('section', 'expert'), may hold values from -0.125 to 0.125
- down_weight: bfloat16 [64, 8, 512, 2048], P('section', 'expert'), may hold values from -0.1875 to 0.1875
Outputs:
- mixed: bfloat16 [65536, 2048], P(('section', 'expert'))
The draws below stay inside these ranges and needn't reach their ends.
Inputs may be any that keep to these rules, and one draw needn't show every extreme that they name: `routes`: each row names 2 different experts; among the rows of one device at one stop, no expert is named by more than 36 rows, a bound that some block reaches.
All inputs are finite; a program needn't handle non-finite values.
Results may differ from the reference program's by a relative error of at most 0.0061.
Values may be sent and summed in bfloat16 or wider, within the bound.
No kernel may reach another device: no remote copies, remote signals or barrier semaphores. Data moves between devices by JAX's collectives and lax.ppermute only.
A program may use at most 64 MiB of HBM per device.

```python
import math
import jax
import jax.numpy as jnp
import numpy as np
from jax import lax

D = 2048
EXP_HID = 1024
TOPK = 2
TICKS = 2
TOK_DEV = 128
EXPERTS = 8
HID_DEV = 512
CAP = 36
TOKENS = 65536
N_SECTION = 64
N_EXPERT = 8


def shard_levels(key, dims, cuts, least, largest):
    factor_of, own = 1.0, jax.random.fold_in(key, 6)
    for position, parts in cuts:
        heights = jnp.exp(jax.random.uniform(jax.random.fold_in(own, position), (parts,), jnp.float32, least / len(cuts), largest / len(cuts)))
        factor_of = factor_of * jnp.repeat(heights, dims[position] // parts).reshape([-1 if axis == position else 1 for axis in range(len(dims))])
    return factor_of


def shared_out(rng, own, number, rows, count, top, reach, skew):
    sequence = jax.random.permutation(rng, count)
    crowded, common = shares(count, rows * top, reach, skew, True), shares(count, rows * top, reach, skew, False)
    places = jnp.arange(count)

    def named(sizes, turn):
        used = int((sizes > 0).sum())
        fixed = max(1, used // 4)
        passed = fixed + (places - fixed + turn * (used - fixed)) % max(1, count - fixed)
        return jnp.zeros((count,), jnp.int32).at[sequence[jnp.where(places < fixed, places, passed)]].set(jnp.asarray(sizes, jnp.int32))

    sizes = jnp.where(number % 4 == 0, named(crowded, number // 4), named(common, number - number // 4 - 1))
    mixed = jax.random.permutation(jax.random.fold_in(own, 3), count)
    source_of, sink = mixed[0:count // 2 * 2:2], mixed[1:count // 2 * 2:2]
    room = jnp.minimum(sizes[source_of] - 1, reach - sizes[sink]) // 2
    room = jnp.where((source_of == sequence[0]) | (sink == sequence[0]) | (sizes[sink] == 0), 0, jnp.maximum(room, 0))
    passed = jax.random.randint(jax.random.fold_in(own, 4), (count // 2,), 0, 1 << 20) % (room + 1)
    sizes = sizes.at[source_of].add(-passed).at[sink].add(passed)
    items = jnp.searchsorted(jnp.cumsum(sizes), jnp.arange(rows * top), side="right").astype(jnp.int32)
    listing = items.reshape(top, rows).T
    listing = listing[jax.random.permutation(jax.random.fold_in(own, 1), rows)]
    turn = jax.random.randint(jax.random.fold_in(own, 2), (rows, 1), 0, top)
    return jnp.take_along_axis(listing, (jnp.arange(top)[None, :] + turn) % top, axis=1)


def shares(amount, total, most, lean, full):
    weights = [(1 << 20) // math.isqrt(grade ** lean) + 1 for grade in range(1, amount + 1)]
    largest = most if full else min(most, max(-(-total // amount), total * weights[0] // sum(weights)))
    least = 1 if total - largest >= amount - 1 else 0
    counts, rest = [largest] + [least] * (amount - 1), total - largest - least * (amount - 1)
    while rest > 0:
        movable = [i for i in range(1, amount) if counts[i] < largest] or [i for i in range(1, amount) if counts[i] < most]
        mass, left = sum([weights[i] for i in movable]), rest
        for i in movable:
            extra = min(most - counts[i], max(1, left * weights[i] // mass), rest)
            counts[i] = counts[i] + extra
            rest = rest - extra
    return np.array(counts)


def scatter_about(stream_key, extent, deviation, most, shards=(), dtype=jnp.bfloat16):
    factor_of = shard_levels(stream_key, extent, shards, -0.22, 0.18) if shards else 1.0
    array = jax.random.normal(stream_key, extent, jnp.float32) * deviation * factor_of
    return jnp.minimum(jnp.maximum(array, -most), most).astype(dtype)


def setup_inputs(seed: int = 0) -> dict:
    streams_of = jax.random.split(jax.random.key(seed), 6)
    tokens = scatter_about(streams_of[0], (TOKENS, D), 1.0, 6.0, ((0, 512),))
    routes_keys = jax.random.split(jax.random.fold_in(streams_of[1], 1), TICKS * TOKENS // TOK_DEV)
    routes_turns = jax.random.permutation(jax.random.fold_in(streams_of[1], 3), TICKS * TOKENS // TOK_DEV)
    routes = jax.vmap(lambda own, number: shared_out(jax.random.fold_in(streams_of[1], 2), own, number, TOK_DEV, EXPERTS, TOPK, CAP, 0))(routes_keys, routes_turns).reshape((TICKS, TOKENS, TOPK))
    combine = jnp.clip(jnp.exp(math.log(4.0) - 2.7725887 * jax.random.uniform(streams_of[2], (TICKS, TOKENS, TOPK), jnp.float32) ** shard_levels(streams_of[2], (TICKS, TOKENS, TOPK), ((1, 512),), -0.2, 0.2)), 0.25, 4.0)
    up_weight = scatter_about(streams_of[3], (N_SECTION, EXPERTS, D, HID_DEV), D ** -0.5, 0.125, ((0, 64), (1, 8)))
    down_weight = scatter_about(streams_of[4], (N_SECTION, EXPERTS, HID_DEV, D), EXP_HID ** -0.5, 0.1875, ((0, 64), (1, 8)))
    return dict(tokens=tokens, routes=routes, combine=combine, up_weight=up_weight, down_weight=down_weight)


def expert_half(rows, up_part, down_part):
    hidden = jax.nn.gelu(jnp.dot(rows, up_part, preferred_element_type=jnp.float32), approximate=True).astype(jnp.bfloat16)
    return jnp.dot(hidden, down_part, preferred_element_type=jnp.float32).astype(jnp.bfloat16)

def layer_pair(args):
    states, ids, weights, ups, downs = args
    states_f = states.astype(jnp.float32)
    normed = (states_f * lax.rsqrt(lax.optimization_barrier(jnp.mean(states_f * states_f, axis=1, keepdims=True)) + 1e-06)).astype(jnp.bfloat16)
    share = weights / lax.optimization_barrier(jnp.sum(weights, axis=1, keepdims=True))
    flat_ids = ids.reshape(-1)
    flat_share = share.reshape(-1)
    limit = 2 * N_EXPERT * CAP
    total = states_f
    for expert_id in range(N_EXPERT):
        order = jnp.argsort((flat_ids != expert_id).astype(jnp.int32), stable=True)[:limit]
        number = jnp.sum((flat_ids == expert_id).astype(jnp.int32))
        source = order // TOPK
        picked = normed[source]
        first = lax.optimization_barrier(expert_half(picked, ups[0, expert_id], downs[0, expert_id]))
        second = lax.optimization_barrier(expert_half(picked, ups[1, expert_id], downs[1, expert_id]))
        summed = (first.astype(jnp.float32) + second.astype(jnp.float32)).astype(jnp.bfloat16)
        summed = lax.optimization_barrier(summed).astype(jnp.float32)
        factor = jnp.where(jnp.arange(limit) < number, flat_share[order], jnp.float32(0.0))
        total = total.at[source].add(factor[:, None] * summed)
    return total.astype(jnp.bfloat16)

def reference(tokens, routes, combine, up_weight, down_weight):
    pair_rows = 2 * N_EXPERT * TOK_DEV
    state = tokens.reshape(N_SECTION, N_EXPERT, TOK_DEV, D)
    ups = up_weight.reshape(N_SECTION // 2, 2, N_EXPERT, D, HID_DEV)
    downs = down_weight.reshape(N_SECTION // 2, 2, N_EXPERT, HID_DEV, D)
    for tick in range(TICKS):
        if tick > 0:
            state = jnp.roll(state, 2, axis=0)
        ids = routes[tick].reshape(N_SECTION // 2, pair_rows, TOPK)
        weights = combine[tick].reshape(N_SECTION // 2, pair_rows, TOPK)
        states = state.reshape(N_SECTION // 2, pair_rows, D)
        state = lax.map(layer_pair, (states, ids, weights, ups, downs)).reshape(N_SECTION, N_EXPERT, TOK_DEV, D)
    return state.reshape(TOKENS, D)
```

```python
import jax
import jax.numpy as jnp
from jax import lax
from jax.sharding import PartitionSpec as P

TICKS = 2


def swapped(value, axis, distance):
    mask = 2**distance
    pairs = [(source, source ^ mask) for source in range(lax.axis_size(axis))]
    return lax.ppermute(value, axis, pairs)


def shifted(value, axis, steps):
    count = lax.axis_size(axis)
    pairs = [(source, (source + steps) % count) for source in range(count)]
    return lax.ppermute(value, axis, pairs)


def expert_half(rows, up_part, down_part):
    hidden = jax.nn.gelu(
        jnp.einsum("gsd,dh->gsh", rows, up_part, preferred_element_type=jnp.float32),
        approximate=True,
    ).astype(jnp.bfloat16)
    return jnp.einsum(
        "gsh,hd->gsd", hidden, down_part, preferred_element_type=jnp.float32
    ).astype(jnp.bfloat16)


def slot_tables(ids, groups, slots):
    rows, top = ids.shape
    flat = ids.reshape(-1)
    count = rows * top
    chosen = (flat[:, None] == jnp.arange(groups, dtype=jnp.int32)[None, :]).astype(jnp.bfloat16)
    earlier = (
        jnp.arange(count, dtype=jnp.int32)[None, :] < jnp.arange(count, dtype=jnp.int32)[:, None]
    ).astype(jnp.bfloat16)
    before = jnp.dot(earlier, chosen, preferred_element_type=jnp.float32)
    position = jnp.sum(before * chosen.astype(jnp.float32), axis=1).astype(jnp.int32)
    position = position.reshape(rows, top)
    group_hit = ids.T[:, None, None, :] == jnp.arange(groups, dtype=jnp.int32)[None, :, None, None]
    slot_hit = position.T[:, None, None, :] == jnp.arange(slots, dtype=jnp.int32)[None, None, :, None]
    return (group_hit & slot_hit).astype(jnp.bfloat16)


def body(tokens, routes, combine, up_weight, down_weight):
    rows = tokens.shape[0]
    top = routes.shape[2]
    groups = lax.axis_size("expert")
    slots = min(rows, rows * top * 9 // (8 * groups))
    up_local = up_weight.reshape(up_weight.shape[2], up_weight.shape[3])
    down_local = down_weight.reshape(down_weight.shape[2], down_weight.shape[3])
    partner_up, partner_down = swapped((up_local, down_local), "section", 0)
    state = tokens
    for tick in range(TICKS):
        if tick > 0:
            state = shifted(state, "section", 2)
        weights = combine[tick]
        select = slot_tables(routes[tick], groups, slots)
        state_f = state.astype(jnp.float32)
        normed = (
            state_f * lax.rsqrt(jnp.mean(state_f * state_f, axis=1, keepdims=True) + 1e-06)
        ).astype(jnp.bfloat16)
        share = weights / jnp.sum(weights, axis=1, keepdims=True)
        dispatch = jnp.sum(select, axis=0)
        outgoing = jnp.einsum(
            "gsr,rd->gsd", dispatch, normed, preferred_element_type=jnp.float32
        ).astype(jnp.bfloat16)
        received = lax.all_to_all(outgoing, "expert", split_axis=0, concat_axis=0, tiled=True)
        own_part = lax.optimization_barrier(expert_half(received, up_local, down_local))
        other_part = lax.optimization_barrier(expert_half(received, partner_up, partner_down))
        summed = own_part.astype(jnp.float32) + other_part.astype(jnp.float32)
        expert_out = summed.astype(jnp.bfloat16)
        answers = lax.all_to_all(expert_out, "expert", split_axis=0, concat_axis=0, tiled=True)
        total = state_f
        for k in range(top):
            picked = jnp.einsum(
                "gsr,gsd->rd", select[k], answers, preferred_element_type=jnp.float32
            )
            total = total + share[:, k : k + 1] * picked
        state = total.astype(jnp.bfloat16)
    return state


def solution(mesh):
    in_specs = (
        P(("section", "expert"), None),
        P(None, ("section", "expert"), None),
        P(None, ("section", "expert"), None),
        P("section", "expert", None, None),
        P("section", "expert", None, None),
    )
    out_specs = P(("section", "expert"), None)
    return jax.shard_map(body, mesh=mesh, in_specs=in_specs, out_specs=out_specs, check_vma=False)
```

```python
import jax
import jax.numpy as jnp
from jax import lax
from jax.experimental import pallas as pl
from jax.experimental.pallas import tpu as pltpu
from jax.sharding import PartitionSpec as P

TICKS = 2


def swapped(value, axis, distance):
    mask = 2**distance
    pairs = [(source, source ^ mask) for source in range(lax.axis_size(axis))]
    return lax.ppermute(value, axis, pairs)


def shifted(value, axis, steps):
    count = lax.axis_size(axis)
    pairs = [(source, (source + steps) % count) for source in range(count)]
    return lax.ppermute(value, axis, pairs)


def expert_kernel(x_ref, own_up, own_down, far_up, far_down, out_ref, half_acc, sum_acc):
    step = pl.program_id(0)
    chunks = pl.num_programs(0) // 2
    half = step // chunks
    chunk = step % chunks

    def partial(up_ref, down_ref):
        hidden = jax.nn.gelu(
            jnp.dot(x_ref[...], up_ref[...], preferred_element_type=jnp.float32), approximate=True
        ).astype(jnp.bfloat16)
        return jnp.dot(hidden, down_ref[...], preferred_element_type=jnp.float32)

    def accumulate(value):
        @pl.when(chunk == 0)
        def _():
            half_acc[...] = value

        @pl.when(chunk > 0)
        def _():
            half_acc[...] += value

    @pl.when(half == 0)
    def _():
        accumulate(partial(own_up, own_down))

    @pl.when(half == 1)
    def _():
        accumulate(partial(far_up, far_down))

    @pl.when((chunk == chunks - 1) & (half == 0))
    def _():
        sum_acc[...] = half_acc[...].astype(jnp.bfloat16).astype(jnp.float32)

    @pl.when((chunk == chunks - 1) & (half == 1))
    def _():
        total = sum_acc[...] + half_acc[...].astype(jnp.bfloat16).astype(jnp.float32)
        out_ref[...] = total.astype(out_ref.dtype)


def expert_full(rows, own_up, own_down, far_up, far_down, chunk=256):
    count, width = rows.shape
    hidden = own_up.shape[1]
    chunks = hidden // chunk
    last = chunks - 1

    def own_col(i):
        return jnp.minimum(i, last)

    def far_col(i):
        return jnp.maximum(i - chunks, 0)

    cost = pl.CostEstimate(
        flops=2 * 2 * count * width * hidden * 2,
        transcendentals=count * hidden * 2,
        bytes_accessed=4 * width * hidden * 2 + 2 * count * width * 2,
    )
    return pl.pallas_call(
        expert_kernel,
        grid=(2 * chunks,),
        in_specs=[
            pl.BlockSpec((count, width), lambda i: (0, 0)),
            pl.BlockSpec((width, chunk), lambda i: (0, own_col(i))),
            pl.BlockSpec((chunk, width), lambda i: (own_col(i), 0)),
            pl.BlockSpec((width, chunk), lambda i: (0, far_col(i))),
            pl.BlockSpec((chunk, width), lambda i: (far_col(i), 0)),
        ],
        out_specs=pl.BlockSpec((count, width), lambda i: (0, 0)),
        out_shape=jax.ShapeDtypeStruct((count, width), jnp.bfloat16),
        scratch_shapes=[
            pltpu.VMEM((count, width), jnp.float32),
            pltpu.VMEM((count, width), jnp.float32),
        ],
        compiler_params=pltpu.CompilerParams(
            dimension_semantics=("arbitrary",), vmem_limit_bytes=48 * 1024 * 1024
        ),
        cost_estimate=cost,
    )(rows, own_up, own_down, far_up, far_down)


def slot_tables(ids, groups, slots):
    rows, top = ids.shape
    flat = ids.reshape(-1)
    count = rows * top
    chosen = (flat[:, None] == jnp.arange(groups, dtype=jnp.int32)[None, :]).astype(jnp.bfloat16)
    earlier = (
        jnp.arange(count, dtype=jnp.int32)[None, :] < jnp.arange(count, dtype=jnp.int32)[:, None]
    ).astype(jnp.bfloat16)
    before = jnp.dot(earlier, chosen, preferred_element_type=jnp.float32)
    position = jnp.sum(before * chosen.astype(jnp.float32), axis=1).astype(jnp.int32)
    position = position.reshape(rows, top)
    group_hit = ids.T[:, None, None, :] == jnp.arange(groups, dtype=jnp.int32)[None, :, None, None]
    slot_hit = position.T[:, None, None, :] == jnp.arange(slots, dtype=jnp.int32)[None, None, :, None]
    return (group_hit & slot_hit).astype(jnp.bfloat16)


def body(tokens, routes, combine, up_weight, down_weight):
    rows = tokens.shape[0]
    top = routes.shape[2]
    groups = lax.axis_size("expert")
    slots = min(rows, rows * top * 9 // (8 * groups))
    slots = -(-slots // 8) * 8
    up_local = up_weight.reshape(up_weight.shape[2], up_weight.shape[3])
    down_local = down_weight.reshape(down_weight.shape[2], down_weight.shape[3])
    partner_up, partner_down = swapped((up_local, down_local), "section", 0)
    state = tokens
    for tick in range(TICKS):
        if tick > 0:
            state = shifted(state, "section", 2)
        weights = combine[tick]
        select = slot_tables(routes[tick], groups, slots)
        state_f = state.astype(jnp.float32)
        normed = (
            state_f * lax.rsqrt(jnp.mean(state_f * state_f, axis=1, keepdims=True) + 1e-06)
        ).astype(jnp.bfloat16)
        share = weights / jnp.sum(weights, axis=1, keepdims=True)
        dispatch = jnp.sum(select, axis=0)
        outgoing = jnp.einsum(
            "gsr,rd->gsd", dispatch, normed, preferred_element_type=jnp.float32
        ).astype(jnp.bfloat16)
        received = lax.all_to_all(outgoing, "expert", split_axis=0, concat_axis=0, tiled=True)
        expert_out = expert_full(
            received.reshape(groups * slots, -1), up_local, down_local, partner_up, partner_down
        ).reshape(groups, slots, -1)
        answers = lax.all_to_all(expert_out, "expert", split_axis=0, concat_axis=0, tiled=True)
        total = state_f
        for k in range(top):
            picked = jnp.einsum(
                "gsr,gsd->rd", select[k], answers, preferred_element_type=jnp.float32
            )
            total = total + share[:, k : k + 1] * picked
        state = total.astype(jnp.bfloat16)
    return state


def solution(mesh):
    in_specs = (
        P(("section", "expert"), None),
        P(None, ("section", "expert"), None),
        P(None, ("section", "expert"), None),
        P("section", "expert", None, None),
        P("section", "expert", None, None),
    )
    out_specs = P(("section", "expert"), None)
    return jax.shard_map(body, mesh=mesh, in_specs=in_specs, out_specs=out_specs, check_vma=False)
```

```python
import functools

import jax
import jax.numpy as jnp
from jax import lax
from jax.experimental import pallas as pl
from jax.experimental.pallas import tpu as pltpu
from jax.sharding import PartitionSpec as P

TICKS = 2


def swapped(value, axis, distance):
    mask = 2**distance
    pairs = [(source, source ^ mask) for source in range(lax.axis_size(axis))]
    return lax.ppermute(value, axis, pairs)


def shifted(value, axis, steps):
    count = lax.axis_size(axis)
    pairs = [(source, (source + steps) % count) for source in range(count)]
    return lax.ppermute(value, axis, pairs)


def expert_kernel(x_ref, own_up_hbm, own_down_hbm, far_up_hbm, far_down_hbm, out_ref,
                  own_up, own_down, far_up, far_down, sems, *, block):
    pairs = ((own_up_hbm, own_up), (far_up_hbm, far_up), (own_down_hbm, own_down), (far_down_hbm, far_down))
    copies = [pltpu.make_async_copy(src, dst, sems.at[i]) for i, (src, dst) in enumerate(pairs)]
    for copy in copies:
        copy.start()
    rows = x_ref[...]

    def hidden_of(up_ref):
        return jax.nn.gelu(
            jnp.dot(rows, up_ref[...], preferred_element_type=jnp.float32), approximate=True
        ).astype(jnp.bfloat16)

    copies[0].wait()
    own_hidden = hidden_of(own_up)
    copies[1].wait()
    far_hidden = hidden_of(far_up)
    copies[2].wait()
    copies[3].wait()
    width = out_ref.shape[1]
    for start in range(0, width, block):
        cols = pl.ds(start, block)
        own_part = jnp.dot(own_hidden, own_down[:, cols], preferred_element_type=jnp.float32)
        far_part = jnp.dot(far_hidden, far_down[:, cols], preferred_element_type=jnp.float32)
        total = own_part.astype(jnp.bfloat16).astype(jnp.float32) + far_part.astype(
            jnp.bfloat16
        ).astype(jnp.float32)
        out_ref[:, cols] = total.astype(out_ref.dtype)


def expert_full(rows, own_up, own_down, far_up, far_down, block=512):
    count, width = rows.shape
    hidden = own_up.shape[1]
    cost = pl.CostEstimate(
        flops=2 * 2 * count * width * hidden * 2,
        transcendentals=count * hidden * 2,
        bytes_accessed=4 * width * hidden * 2 + 2 * count * width * 2,
    )
    weight = pl.BlockSpec(memory_space=pl.ANY)
    return pl.pallas_call(
        functools.partial(expert_kernel, block=block),
        in_specs=[pl.BlockSpec(memory_space=pltpu.VMEM), weight, weight, weight, weight],
        out_specs=pl.BlockSpec(memory_space=pltpu.VMEM),
        out_shape=jax.ShapeDtypeStruct((count, width), jnp.bfloat16),
        scratch_shapes=[
            pltpu.VMEM(own_up.shape, own_up.dtype),
            pltpu.VMEM(own_down.shape, own_down.dtype),
            pltpu.VMEM(far_up.shape, far_up.dtype),
            pltpu.VMEM(far_down.shape, far_down.dtype),
            pltpu.SemaphoreType.DMA((4,)),
        ],
        compiler_params=pltpu.CompilerParams(vmem_limit_bytes=48 * 1024 * 1024),
        cost_estimate=cost,
    )(rows, own_up, own_down, far_up, far_down)


def slot_tables(ids, groups, slots):
    rows, top = ids.shape
    flat = ids.reshape(-1)
    count = rows * top
    chosen = (flat[:, None] == jnp.arange(groups, dtype=jnp.int32)[None, :]).astype(jnp.bfloat16)
    earlier = (
        jnp.arange(count, dtype=jnp.int32)[None, :] < jnp.arange(count, dtype=jnp.int32)[:, None]
    ).astype(jnp.bfloat16)
    before = jnp.dot(earlier, chosen, preferred_element_type=jnp.float32)
    position = jnp.sum(before * chosen.astype(jnp.float32), axis=1).astype(jnp.int32)
    position = position.reshape(rows, top)
    group_hit = ids.T[:, None, None, :] == jnp.arange(groups, dtype=jnp.int32)[None, :, None, None]
    slot_hit = position.T[:, None, None, :] == jnp.arange(slots, dtype=jnp.int32)[None, None, :, None]
    return (group_hit & slot_hit).astype(jnp.bfloat16)


def body(tokens, routes, combine, up_weight, down_weight):
    rows = tokens.shape[0]
    top = routes.shape[2]
    groups = lax.axis_size("expert")
    slots = min(rows, rows * top * 9 // (8 * groups))
    slots = -(-slots // 8) * 8
    up_local = up_weight.reshape(up_weight.shape[2], up_weight.shape[3])
    down_local = down_weight.reshape(down_weight.shape[2], down_weight.shape[3])
    partner_up, partner_down = swapped((up_local, down_local), "section", 0)
    state = tokens
    for tick in range(TICKS):
        if tick > 0:
            state = shifted(state, "section", 2)
        weights = combine[tick]
        select = slot_tables(routes[tick], groups, slots)
        state_f = state.astype(jnp.float32)
        normed = (
            state_f * lax.rsqrt(jnp.mean(state_f * state_f, axis=1, keepdims=True) + 1e-06)
        ).astype(jnp.bfloat16)
        share = weights / jnp.sum(weights, axis=1, keepdims=True)
        dispatch = jnp.sum(select, axis=0)
        outgoing = jnp.einsum(
            "gsr,rd->gsd", dispatch, normed, preferred_element_type=jnp.float32
        ).astype(jnp.bfloat16)
        received = lax.all_to_all(outgoing, "expert", split_axis=0, concat_axis=0, tiled=True)
        expert_out = expert_full(
            received.reshape(groups * slots, -1), up_local, down_local, partner_up, partner_down
        ).reshape(groups, slots, -1)
        answers = lax.all_to_all(expert_out, "expert", split_axis=0, concat_axis=0, tiled=True)
        total = state_f
        for k in range(top):
            picked = jnp.einsum(
                "gsr,gsd->rd", select[k], answers, preferred_element_type=jnp.float32
            )
            total = total + share[:, k : k + 1] * picked
        state = total.astype(jnp.bfloat16)
    return state


def solution(mesh):
    in_specs = (
        P(("section", "expert"), None),
        P(None, ("section", "expert"), None),
        P(None, ("section", "expert"), None),
        P("section", "expert", None, None),
        P("section", "expert", None, None),
    )
    out_specs = P(("section", "expert"), None)
    return jax.shard_map(body, mesh=mesh, in_specs=in_specs, out_specs=out_specs, check_vma=False)
```

```python
import functools

import jax
import jax.numpy as jnp
from jax import lax
from jax.experimental import pallas as pl
from jax.experimental.pallas import tpu as pltpu
from jax.sharding import PartitionSpec as P

TICKS = 2


def swapped(value, axis, distance):
    mask = 2**distance
    pairs = [(source, source ^ mask) for source in range(lax.axis_size(axis))]
    return lax.ppermute(value, axis, pairs)


def shifted(value, axis, steps):
    count = lax.axis_size(axis)
    pairs = [(source, (source + steps) % count) for source in range(count)]
    return lax.ppermute(value, axis, pairs)


def expert_kernel(x_ref, own_up_hbm, own_down_hbm, far_up_hbm, far_down_hbm, out_ref,
                  own_up, own_down, far_up, far_down, sems, *, block):
    pairs = ((own_up_hbm, own_up), (far_up_hbm, far_up), (own_down_hbm, own_down), (far_down_hbm, far_down))
    copies = [pltpu.make_async_copy(src, dst, sems.at[i]) for i, (src, dst) in enumerate(pairs)]
    for copy in copies:
        copy.start()
    rows = x_ref[...]

    def hidden_of(up_ref):
        return jax.nn.gelu(
            jnp.dot(rows, up_ref[...], preferred_element_type=jnp.float32), approximate=True
        ).astype(jnp.bfloat16)

    copies[0].wait()
    own_hidden = hidden_of(own_up)
    copies[1].wait()
    far_hidden = hidden_of(far_up)
    copies[2].wait()
    copies[3].wait()
    width = out_ref.shape[1]
    for start in range(0, width, block):
        cols = pl.ds(start, block)
        own_part = jnp.dot(own_hidden, own_down[:, cols], preferred_element_type=jnp.float32)
        far_part = jnp.dot(far_hidden, far_down[:, cols], preferred_element_type=jnp.float32)
        total = own_part.astype(jnp.bfloat16).astype(jnp.float32) + far_part.astype(
            jnp.bfloat16
        ).astype(jnp.float32)
        out_ref[:, cols] = total.astype(out_ref.dtype)


def expert_full(rows, own_up, own_down, far_up, far_down, block=512):
    count, width = rows.shape
    hidden = own_up.shape[1]
    cost = pl.CostEstimate(
        flops=2 * 2 * count * width * hidden * 2,
        transcendentals=count * hidden * 2,
        bytes_accessed=4 * width * hidden * 2 + 2 * count * width * 2,
    )
    weight = pl.BlockSpec(memory_space=pl.ANY)
    return pl.pallas_call(
        functools.partial(expert_kernel, block=block),
        in_specs=[pl.BlockSpec(memory_space=pltpu.VMEM), weight, weight, weight, weight],
        out_specs=pl.BlockSpec(memory_space=pltpu.VMEM),
        out_shape=jax.ShapeDtypeStruct((count, width), jnp.bfloat16),
        scratch_shapes=[
            pltpu.VMEM(own_up.shape, own_up.dtype),
            pltpu.VMEM(own_down.shape, own_down.dtype),
            pltpu.VMEM(far_up.shape, far_up.dtype),
            pltpu.VMEM(far_down.shape, far_down.dtype),
            pltpu.SemaphoreType.DMA((4,)),
        ],
        compiler_params=pltpu.CompilerParams(vmem_limit_bytes=48 * 1024 * 1024),
        cost_estimate=cost,
    )(rows, own_up, own_down, far_up, far_down)


def dispatch_kernel(state_ref, select_ref, out_ref):
    state = state_ref[...].astype(jnp.float32)
    scale = lax.rsqrt(jnp.mean(state * state, axis=1, keepdims=True) + 1e-06)
    normed = (state * scale).astype(jnp.bfloat16)
    out_ref[...] = jnp.dot(select_ref[...], normed, preferred_element_type=jnp.float32).astype(
        out_ref.dtype
    )


def dispatch_rows(state, select):
    count = select.shape[0]
    width = state.shape[1]
    vmem = pl.BlockSpec(memory_space=pltpu.VMEM)
    return pl.pallas_call(
        dispatch_kernel,
        in_specs=[vmem, vmem],
        out_specs=vmem,
        out_shape=jax.ShapeDtypeStruct((count, width), jnp.bfloat16),
        cost_estimate=pl.CostEstimate(
            flops=2 * count * state.shape[0] * width,
            transcendentals=state.shape[0],
            bytes_accessed=2 * (count + state.shape[0]) * width,
        ),
    )(state, select)


def combine_kernel(state_ref, answers_ref, pick_ref, share_ref, out_ref):
    total = state_ref[...].astype(jnp.float32)
    answers = answers_ref[...]
    for k in range(pick_ref.shape[0]):
        picked = jnp.dot(pick_ref[k], answers, preferred_element_type=jnp.float32)
        total = total + share_ref[:, k : k + 1] * picked
    out_ref[...] = total.astype(out_ref.dtype)


def combine_rows(state, answers, pick, share):
    rows, width = state.shape
    vmem = pl.BlockSpec(memory_space=pltpu.VMEM)
    return pl.pallas_call(
        combine_kernel,
        in_specs=[vmem, vmem, vmem, vmem],
        out_specs=vmem,
        out_shape=jax.ShapeDtypeStruct((rows, width), state.dtype),
        cost_estimate=pl.CostEstimate(
            flops=2 * pick.shape[0] * rows * answers.shape[0] * width,
            transcendentals=0,
            bytes_accessed=2 * (2 * rows + answers.shape[0]) * width,
        ),
    )(state, answers, pick, share)


def slot_tables(ids, groups, slots):
    rows, top = ids.shape
    flat = ids.reshape(-1)
    count = rows * top
    chosen = (flat[:, None] == jnp.arange(groups, dtype=jnp.int32)[None, :]).astype(jnp.bfloat16)
    earlier = (
        jnp.arange(count, dtype=jnp.int32)[None, :] < jnp.arange(count, dtype=jnp.int32)[:, None]
    ).astype(jnp.bfloat16)
    before = jnp.dot(earlier, chosen, preferred_element_type=jnp.float32)
    position = jnp.sum(before * chosen.astype(jnp.float32), axis=1).astype(jnp.int32)
    position = position.reshape(rows, top)
    group_hit = ids.T[:, None, None, :] == jnp.arange(groups, dtype=jnp.int32)[None, :, None, None]
    slot_hit = position.T[:, None, None, :] == jnp.arange(slots, dtype=jnp.int32)[None, None, :, None]
    return (group_hit & slot_hit).astype(jnp.bfloat16)


def body(tokens, routes, combine, up_weight, down_weight):
    rows = tokens.shape[0]
    top = routes.shape[2]
    groups = lax.axis_size("expert")
    slots = min(rows, rows * top * 9 // (8 * groups))
    slots = -(-slots // 8) * 8
    up_local = up_weight.reshape(up_weight.shape[2], up_weight.shape[3])
    down_local = down_weight.reshape(down_weight.shape[2], down_weight.shape[3])
    partner_up, partner_down = swapped((up_local, down_local), "section", 0)
    state = tokens
    for tick in range(TICKS):
        if tick > 0:
            state = shifted(state, "section", 2)
        weights = combine[tick]
        select = slot_tables(routes[tick], groups, slots)
        share = weights / jnp.sum(weights, axis=1, keepdims=True)
        dispatch = jnp.sum(select, axis=0).reshape(groups * slots, rows)
        outgoing = dispatch_rows(state, dispatch).reshape(groups, slots, -1)
        received = lax.all_to_all(outgoing, "expert", split_axis=0, concat_axis=0, tiled=True)
        expert_out = expert_full(
            received.reshape(groups * slots, -1), up_local, down_local, partner_up, partner_down
        ).reshape(groups, slots, -1)
        answers = lax.all_to_all(expert_out, "expert", split_axis=0, concat_axis=0, tiled=True)
        pick = jnp.swapaxes(select.reshape(top, groups * slots, rows), 1, 2)
        state = combine_rows(state, answers.reshape(groups * slots, -1), pick, share)
    return state


def solution(mesh):
    in_specs = (
        P(("section", "expert"), None),
        P(None, ("section", "expert"), None),
        P(None, ("section", "expert"), None),
        P("section", "expert", None, None),
        P("section", "expert", None, None),
    )
    out_specs = P(("section", "expert"), None)
    return jax.shard_map(body, mesh=mesh, in_specs=in_specs, out_specs=out_specs, check_vma=False)
```

```python
import functools

import jax
import jax.numpy as jnp
from jax import lax
from jax.experimental import pallas as pl
from jax.experimental.pallas import tpu as pltpu
from jax.sharding import PartitionSpec as P

TICKS = 2


def swapped(value, axis, distance):
    mask = 2**distance
    pairs = [(source, source ^ mask) for source in range(lax.axis_size(axis))]
    return lax.ppermute(value, axis, pairs)


def shifted(value, axis, steps):
    count = lax.axis_size(axis)
    pairs = [(source, (source + steps) % count) for source in range(count)]
    return lax.ppermute(value, axis, pairs)


def expert_kernel(x_ref, own_up_hbm, own_down_hbm, far_up_hbm, far_down_hbm, out_ref,
                  own_up, own_down, far_up, far_down, sems, *, block):
    pairs = ((own_up_hbm, own_up), (far_up_hbm, far_up), (own_down_hbm, own_down), (far_down_hbm, far_down))
    copies = [pltpu.make_async_copy(src, dst, sems.at[i]) for i, (src, dst) in enumerate(pairs)]
    for copy in copies:
        copy.start()
    rows = x_ref[...]

    def hidden_of(up_ref):
        return jax.nn.gelu(
            jnp.dot(rows, up_ref[...], preferred_element_type=jnp.float32), approximate=True
        ).astype(jnp.bfloat16)

    copies[0].wait()
    own_hidden = hidden_of(own_up)
    copies[1].wait()
    far_hidden = hidden_of(far_up)
    copies[2].wait()
    copies[3].wait()
    width = out_ref.shape[1]
    for start in range(0, width, block):
        cols = pl.ds(start, block)
        own_part = jnp.dot(own_hidden, own_down[:, cols], preferred_element_type=jnp.float32)
        far_part = jnp.dot(far_hidden, far_down[:, cols], preferred_element_type=jnp.float32)
        total = own_part.astype(jnp.bfloat16).astype(jnp.float32) + far_part.astype(
            jnp.bfloat16
        ).astype(jnp.float32)
        out_ref[:, cols] = total.astype(out_ref.dtype)


def expert_full(rows, own_up, own_down, far_up, far_down, block=512):
    count, width = rows.shape
    hidden = own_up.shape[1]
    cost = pl.CostEstimate(
        flops=2 * 2 * count * width * hidden * 2,
        transcendentals=count * hidden * 2,
        bytes_accessed=4 * width * hidden * 2 + 2 * count * width * 2,
    )
    weight = pl.BlockSpec(memory_space=pl.ANY)
    return pl.pallas_call(
        functools.partial(expert_kernel, block=block),
        in_specs=[pl.BlockSpec(memory_space=pltpu.VMEM), weight, weight, weight, weight],
        out_specs=pl.BlockSpec(memory_space=pltpu.VMEM),
        out_shape=jax.ShapeDtypeStruct((count, width), jnp.bfloat16),
        scratch_shapes=[
            pltpu.VMEM(own_up.shape, own_up.dtype),
            pltpu.VMEM(own_down.shape, own_down.dtype),
            pltpu.VMEM(far_up.shape, far_up.dtype),
            pltpu.VMEM(far_down.shape, far_down.dtype),
            pltpu.SemaphoreType.DMA((4,)),
        ],
        compiler_params=pltpu.CompilerParams(vmem_limit_bytes=48 * 1024 * 1024),
        cost_estimate=cost,
    )(rows, own_up, own_down, far_up, far_down)


def slot_tables(ids, groups, slots):
    rows, top = ids.shape
    flat = ids.reshape(-1)
    count = rows * top
    chosen = (flat[:, None] == jnp.arange(groups, dtype=jnp.int32)[None, :]).astype(jnp.bfloat16)
    earlier = (
        jnp.arange(count, dtype=jnp.int32)[None, :] < jnp.arange(count, dtype=jnp.int32)[:, None]
    ).astype(jnp.bfloat16)
    before = jnp.dot(earlier, chosen, preferred_element_type=jnp.float32)
    position = jnp.sum(before * chosen.astype(jnp.float32), axis=1).astype(jnp.int32)
    position = position.reshape(rows, top)
    group_hit = ids.T[:, None, None, :] == jnp.arange(groups, dtype=jnp.int32)[None, :, None, None]
    slot_hit = position.T[:, None, None, :] == jnp.arange(slots, dtype=jnp.int32)[None, None, :, None]
    return (group_hit & slot_hit).astype(jnp.bfloat16)


def body(tokens, routes, combine, up_weight, down_weight):
    rows = tokens.shape[0]
    top = routes.shape[2]
    groups = lax.axis_size("expert")
    slots = min(rows, rows * top * 9 // (8 * groups))
    slots = -(-slots // 8) * 8
    up_local = up_weight.reshape(up_weight.shape[2], up_weight.shape[3])
    down_local = down_weight.reshape(down_weight.shape[2], down_weight.shape[3])
    partner_up, partner_down = swapped((up_local, down_local), "section", 0)
    state = tokens
    for tick in range(TICKS):
        if tick > 0:
            state = shifted(state, "section", 2)
        weights = combine[tick]
        select = slot_tables(routes[tick], groups, slots)
        state_f = state.astype(jnp.float32)
        gram = jnp.dot(state, state.T, preferred_element_type=jnp.float32)
        eye = jnp.arange(rows)[:, None] == jnp.arange(rows)[None, :]
        squares = jnp.sum(jnp.where(eye, gram, 0.0), axis=1, keepdims=True)
        normed = (state_f * lax.rsqrt(squares / state.shape[1] + 1e-06)).astype(jnp.bfloat16)
        share = weights / jnp.sum(weights, axis=1, keepdims=True)
        dispatch = jnp.sum(select, axis=0)
        outgoing = jnp.einsum(
            "gsr,rd->gsd", dispatch, normed, preferred_element_type=jnp.float32
        ).astype(jnp.bfloat16)
        received = lax.all_to_all(outgoing, "expert", split_axis=0, concat_axis=0, tiled=True)
        expert_out = expert_full(
            received.reshape(groups * slots, -1), up_local, down_local, partner_up, partner_down
        ).reshape(groups, slots, -1)
        answers = lax.all_to_all(expert_out, "expert", split_axis=0, concat_axis=0, tiled=True)
        total = state_f
        for k in range(top):
            picked = jnp.einsum(
                "gsr,gsd->rd", select[k], answers, preferred_element_type=jnp.float32
            )
            total = total + share[:, k : k + 1] * picked
        state = total.astype(jnp.bfloat16)
    return state


def solution(mesh):
    in_specs = (
        P(("section", "expert"), None),
        P(None, ("section", "expert"), None),
        P(None, ("section", "expert"), None),
        P("section", "expert", None, None),
        P("section", "expert", None, None),
    )
    out_specs = P(("section", "expert"), None)
    return jax.shard_map(body, mesh=mesh, in_specs=in_specs, out_specs=out_specs, check_vma=False)
```

```python
import functools

import jax
import jax.numpy as jnp
from jax import lax
from jax.experimental import pallas as pl
from jax.experimental.pallas import tpu as pltpu
from jax.sharding import PartitionSpec as P

TICKS = 2


def swapped(value, axis, distance):
    mask = 2**distance
    pairs = [(source, source ^ mask) for source in range(lax.axis_size(axis))]
    return lax.ppermute(value, axis, pairs)


def shifted(value, axis, steps):
    count = lax.axis_size(axis)
    pairs = [(source, (source + steps) % count) for source in range(count)]
    return lax.ppermute(value, axis, pairs)


def expert_kernel(x_ref, own_up_hbm, own_down_hbm, far_up_hbm, far_down_hbm, out_ref,
                  own_up, own_down, far_up, far_down, sems, *, block):
    pairs = ((own_up_hbm, own_up), (far_up_hbm, far_up), (own_down_hbm, own_down), (far_down_hbm, far_down))
    copies = [pltpu.make_async_copy(src, dst, sems.at[i]) for i, (src, dst) in enumerate(pairs)]
    for copy in copies:
        copy.start()
    rows = x_ref[...]

    def hidden_of(up_ref):
        return jax.nn.gelu(
            jnp.dot(rows, up_ref[...], preferred_element_type=jnp.float32), approximate=True
        ).astype(jnp.bfloat16)

    copies[0].wait()
    own_hidden = hidden_of(own_up)
    copies[1].wait()
    far_hidden = hidden_of(far_up)
    copies[2].wait()
    copies[3].wait()
    width = out_ref.shape[1]
    for start in range(0, width, block):
        cols = pl.ds(start, block)
        own_part = jnp.dot(own_hidden, own_down[:, cols], preferred_element_type=jnp.float32)
        far_part = jnp.dot(far_hidden, far_down[:, cols], preferred_element_type=jnp.float32)
        total = own_part.astype(jnp.bfloat16).astype(jnp.float32) + far_part.astype(
            jnp.bfloat16
        ).astype(jnp.float32)
        out_ref[:, cols] = total.astype(out_ref.dtype)


def expert_full(rows, own_up, own_down, far_up, far_down, block=512):
    count, width = rows.shape
    hidden = own_up.shape[1]
    cost = pl.CostEstimate(
        flops=2 * 2 * count * width * hidden * 2,
        transcendentals=count * hidden * 2,
        bytes_accessed=4 * width * hidden * 2 + 2 * count * width * 2,
    )
    weight = pl.BlockSpec(memory_space=pl.ANY)
    return pl.pallas_call(
        functools.partial(expert_kernel, block=block),
        in_specs=[pl.BlockSpec(memory_space=pltpu.VMEM), weight, weight, weight, weight],
        out_specs=pl.BlockSpec(memory_space=pltpu.VMEM),
        out_shape=jax.ShapeDtypeStruct((count, width), jnp.bfloat16),
        scratch_shapes=[
            pltpu.VMEM(own_up.shape, own_up.dtype),
            pltpu.VMEM(own_down.shape, own_down.dtype),
            pltpu.VMEM(far_up.shape, far_up.dtype),
            pltpu.VMEM(far_down.shape, far_down.dtype),
            pltpu.SemaphoreType.DMA((4,)),
        ],
        compiler_params=pltpu.CompilerParams(vmem_limit_bytes=48 * 1024 * 1024),
        cost_estimate=cost,
    )(rows, own_up, own_down, far_up, far_down)


def slot_tables(ids, groups, slots):
    rows, top = ids.shape
    by_choice = ids.T
    flat = by_choice.reshape(-1)
    count = rows * top
    chosen = (flat[:, None] == jnp.arange(groups, dtype=jnp.int32)[None, :]).astype(jnp.bfloat16)
    earlier = (
        jnp.arange(count, dtype=jnp.int32)[None, :] < jnp.arange(count, dtype=jnp.int32)[:, None]
    ).astype(jnp.bfloat16)
    before = jnp.dot(earlier, chosen, preferred_element_type=jnp.float32)
    position = jnp.sum(before * chosen.astype(jnp.float32), axis=1).astype(jnp.int32)
    position = position.reshape(top, rows)
    group_hit = by_choice[:, None, None, :] == jnp.arange(groups, dtype=jnp.int32)[None, :, None, None]
    slot_hit = position[:, None, None, :] == jnp.arange(slots, dtype=jnp.int32)[None, None, :, None]
    return (group_hit & slot_hit).astype(jnp.bfloat16)


def body(tokens, routes, combine, up_weight, down_weight):
    rows = tokens.shape[0]
    top = routes.shape[2]
    groups = lax.axis_size("expert")
    slots = min(rows, rows * top * 9 // (8 * groups))
    slots = -(-slots // 8) * 8
    up_local = up_weight.reshape(up_weight.shape[2], up_weight.shape[3])
    down_local = down_weight.reshape(down_weight.shape[2], down_weight.shape[3])
    partner_up, partner_down = swapped((up_local, down_local), "section", 0)
    state = tokens
    for tick in range(TICKS):
        if tick > 0:
            state = shifted(state, "section", 2)
        weights = combine[tick]
        select = slot_tables(routes[tick], groups, slots)
        state_f = state.astype(jnp.float32)
        normed = (
            state_f * lax.rsqrt(jnp.mean(state_f * state_f, axis=1, keepdims=True) + 1e-06)
        ).astype(jnp.bfloat16)
        share = weights / jnp.sum(weights, axis=1, keepdims=True)
        dispatch = jnp.sum(select, axis=0)
        outgoing = jnp.einsum(
            "gsr,rd->gsd", dispatch, normed, preferred_element_type=jnp.float32
        ).astype(jnp.bfloat16)
        received = lax.all_to_all(outgoing, "expert", split_axis=0, concat_axis=0, tiled=True)
        expert_out = expert_full(
            received.reshape(groups * slots, -1), up_local, down_local, partner_up, partner_down
        ).reshape(groups, slots, -1)
        answers = lax.all_to_all(expert_out, "expert", split_axis=0, concat_axis=0, tiled=True)
        total = state_f
        for k in range(top):
            picked = jnp.einsum(
                "gsr,gsd->rd", select[k], answers, preferred_element_type=jnp.float32
            )
            total = total + share[:, k : k + 1] * picked
        state = total.astype(jnp.bfloat16)
    return state


def solution(mesh):
    in_specs = (
        P(("section", "expert"), None),
        P(None, ("section", "expert"), None),
        P(None, ("section", "expert"), None),
        P("section", "expert", None, None),
        P("section", "expert", None, None),
    )
    out_specs = P(("section", "expert"), None)
    return jax.shard_map(body, mesh=mesh, in_specs=in_specs, out_specs=out_specs, check_vma=False)
```

```python
import functools

import jax
import jax.numpy as jnp
from jax import lax
from jax.experimental import pallas as pl
from jax.experimental.pallas import tpu as pltpu
from jax.sharding import PartitionSpec as P

TICKS = 2


def swapped(value, axis, distance):
    mask = 2**distance
    pairs = [(source, source ^ mask) for source in range(lax.axis_size(axis))]
    return lax.ppermute(value, axis, pairs)


def shifted(value, axis, steps):
    count = lax.axis_size(axis)
    pairs = [(source, (source + steps) % count) for source in range(count)]
    return lax.ppermute(value, axis, pairs)


def expert_kernel(x_ref, own_up_hbm, own_down_hbm, far_up_hbm, far_down_hbm, out_ref,
                  own_up, own_down, far_up, far_down, sems, *, block):
    pairs = ((own_up_hbm, own_up), (far_up_hbm, far_up), (own_down_hbm, own_down), (far_down_hbm, far_down))
    copies = [pltpu.make_async_copy(src, dst, sems.at[i]) for i, (src, dst) in enumerate(pairs)]
    for copy in copies:
        copy.start()
    rows = x_ref[...]

    def hidden_of(up_ref):
        return jax.nn.gelu(
            jnp.dot(rows, up_ref[...], preferred_element_type=jnp.float32), approximate=True
        ).astype(jnp.bfloat16)

    copies[0].wait()
    own_hidden = hidden_of(own_up)
    copies[1].wait()
    far_hidden = hidden_of(far_up)
    copies[2].wait()
    copies[3].wait()
    width = out_ref.shape[1]
    for start in range(0, width, block):
        cols = pl.ds(start, block)
        own_part = jnp.dot(own_hidden, own_down[:, cols], preferred_element_type=jnp.float32)
        far_part = jnp.dot(far_hidden, far_down[:, cols], preferred_element_type=jnp.float32)
        total = own_part.astype(jnp.bfloat16).astype(jnp.float32) + far_part.astype(
            jnp.bfloat16
        ).astype(jnp.float32)
        out_ref[:, cols] = total.astype(out_ref.dtype)


def expert_full(rows, own_up, own_down, far_up, far_down, block=512):
    count, width = rows.shape
    hidden = own_up.shape[1]
    cost = pl.CostEstimate(
        flops=2 * 2 * count * width * hidden * 2,
        transcendentals=count * hidden * 2,
        bytes_accessed=4 * width * hidden * 2 + 2 * count * width * 2,
    )
    weight = pl.BlockSpec(memory_space=pl.ANY)
    return pl.pallas_call(
        functools.partial(expert_kernel, block=block),
        in_specs=[pl.BlockSpec(memory_space=pltpu.VMEM), weight, weight, weight, weight],
        out_specs=pl.BlockSpec(memory_space=pltpu.VMEM),
        out_shape=jax.ShapeDtypeStruct((count, width), jnp.bfloat16),
        scratch_shapes=[
            pltpu.VMEM(own_up.shape, own_up.dtype),
            pltpu.VMEM(own_down.shape, own_down.dtype),
            pltpu.VMEM(far_up.shape, far_up.dtype),
            pltpu.VMEM(far_down.shape, far_down.dtype),
            pltpu.SemaphoreType.DMA((4,)),
        ],
        compiler_params=pltpu.CompilerParams(vmem_limit_bytes=48 * 1024 * 1024),
        cost_estimate=cost,
    )(rows, own_up, own_down, far_up, far_down)


def slot_tables(ids, groups, slots):
    rows, top = ids.shape
    flat = ids.reshape(-1)
    count = rows * top
    chosen = (flat[:, None] == jnp.arange(groups, dtype=jnp.int32)[None, :]).astype(jnp.bfloat16)
    earlier = (
        jnp.arange(count, dtype=jnp.int32)[None, :] < jnp.arange(count, dtype=jnp.int32)[:, None]
    ).astype(jnp.bfloat16)
    before = jnp.dot(earlier, chosen, preferred_element_type=jnp.float32)
    position = jnp.sum(before * chosen.astype(jnp.float32), axis=1).astype(jnp.int32)
    position = position.reshape(rows, top)
    group_hit = ids.T[:, None, None, :] == jnp.arange(groups, dtype=jnp.int32)[None, :, None, None]
    slot_hit = position.T[:, None, None, :] == jnp.arange(slots, dtype=jnp.int32)[None, None, :, None]
    return (group_hit & slot_hit).astype(jnp.bfloat16)


def body(tokens, routes, combine, up_weight, down_weight):
    rows = tokens.shape[0]
    top = routes.shape[2]
    groups = lax.axis_size("expert")
    slots = min(rows, rows * top * 9 // (8 * groups))
    slots = -(-slots // 8) * 8
    up_local = up_weight.reshape(up_weight.shape[2], up_weight.shape[3])
    down_local = down_weight.reshape(down_weight.shape[2], down_weight.shape[3])
    state = tokens
    for tick in range(TICKS):
        if tick > 0:
            state = shifted(state, "section", 2)
        weights = combine[tick]
        select = slot_tables(routes[tick], groups, slots)
        state_f = state.astype(jnp.float32)
        normed = (
            state_f * lax.rsqrt(jnp.mean(state_f * state_f, axis=1, keepdims=True) + 1e-06)
        ).astype(jnp.bfloat16)
        share = weights / jnp.sum(weights, axis=1, keepdims=True)
        dispatch = jnp.sum(select, axis=0)
        outgoing = jnp.einsum(
            "gsr,rd->gsd", dispatch, normed, preferred_element_type=jnp.float32
        ).astype(jnp.bfloat16)
        if tick == 0:
            outgoing, up_local, down_local = lax.optimization_barrier(
                (outgoing, up_local, down_local)
            )
            partner_up, partner_down = swapped((up_local, down_local), "section", 0)
        received = lax.all_to_all(outgoing, "expert", split_axis=0, concat_axis=0, tiled=True)
        expert_out = expert_full(
            received.reshape(groups * slots, -1), up_local, down_local, partner_up, partner_down
        ).reshape(groups, slots, -1)
        answers = lax.all_to_all(expert_out, "expert", split_axis=0, concat_axis=0, tiled=True)
        total = state_f
        for k in range(top):
            picked = jnp.einsum(
                "gsr,gsd->rd", select[k], answers, preferred_element_type=jnp.float32
            )
            total = total + share[:, k : k + 1] * picked
        state = total.astype(jnp.bfloat16)
    return state


def solution(mesh):
    in_specs = (
        P(("section", "expert"), None),
        P(None, ("section", "expert"), None),
        P(None, ("section", "expert"), None),
        P("section", "expert", None, None),
        P("section", "expert", None, None),
    )
    out_specs = P(("section", "expert"), None)
    return jax.shard_map(body, mesh=mesh, in_specs=in_specs, out_specs=out_specs, check_vma=False)
```

```python
import functools

import jax
import jax.numpy as jnp
from jax import lax
from jax.experimental import pallas as pl
from jax.experimental.pallas import tpu as pltpu
from jax.sharding import PartitionSpec as P

TICKS = 2


def swapped(value, axis, distance):
    mask = 2**distance
    pairs = [(source, source ^ mask) for source in range(lax.axis_size(axis))]
    return lax.ppermute(value, axis, pairs)


def shifted(value, axis, steps):
    count = lax.axis_size(axis)
    pairs = [(source, (source + steps) % count) for source in range(count)]
    return lax.ppermute(value, axis, pairs)


def expert_kernel(x_ref, own_up_hbm, own_down_hbm, far_up_hbm, far_down_hbm, out_ref,
                  own_up, own_down, far_up, far_down, sems, *, block):
    pairs = ((own_up_hbm, own_up), (far_up_hbm, far_up), (own_down_hbm, own_down), (far_down_hbm, far_down))
    copies = [pltpu.make_async_copy(src, dst, sems.at[i]) for i, (src, dst) in enumerate(pairs)]
    for copy in copies:
        copy.start()
    rows = x_ref[...]

    def hidden_of(up_ref):
        return jax.nn.gelu(
            jnp.dot(rows, up_ref[...], preferred_element_type=jnp.float32), approximate=True
        ).astype(jnp.bfloat16)

    copies[0].wait()
    own_hidden = hidden_of(own_up)
    copies[1].wait()
    far_hidden = hidden_of(far_up)
    copies[2].wait()
    copies[3].wait()
    width = out_ref.shape[1]
    for start in range(0, width, block):
        cols = pl.ds(start, block)
        own_part = jnp.dot(own_hidden, own_down[:, cols], preferred_element_type=jnp.float32)
        far_part = jnp.dot(far_hidden, far_down[:, cols], preferred_element_type=jnp.float32)
        total = own_part.astype(jnp.bfloat16).astype(jnp.float32) + far_part.astype(
            jnp.bfloat16
        ).astype(jnp.float32)
        out_ref[:, cols] = total.astype(out_ref.dtype)


def expert_full(rows, own_up, own_down, far_up, far_down, block=512):
    count, width = rows.shape
    hidden = own_up.shape[1]
    cost = pl.CostEstimate(
        flops=2 * 2 * count * width * hidden * 2,
        transcendentals=count * hidden * 2,
        bytes_accessed=4 * width * hidden * 2 + 2 * count * width * 2,
    )
    weight = pl.BlockSpec(memory_space=pl.ANY)
    return pl.pallas_call(
        functools.partial(expert_kernel, block=block),
        in_specs=[pl.BlockSpec(memory_space=pltpu.VMEM), weight, weight, weight, weight],
        out_specs=pl.BlockSpec(memory_space=pltpu.VMEM),
        out_shape=jax.ShapeDtypeStruct((count, width), jnp.bfloat16),
        scratch_shapes=[
            pltpu.VMEM(own_up.shape, own_up.dtype),
            pltpu.VMEM(own_down.shape, own_down.dtype),
            pltpu.VMEM(far_up.shape, far_up.dtype),
            pltpu.VMEM(far_down.shape, far_down.dtype),
            pltpu.SemaphoreType.DMA((4,)),
        ],
        compiler_params=pltpu.CompilerParams(vmem_limit_bytes=24 * 1024 * 1024),
        cost_estimate=cost,
    )(rows, own_up, own_down, far_up, far_down)


def slot_tables(ids, groups, slots):
    rows, top = ids.shape
    flat = ids.reshape(-1)
    count = rows * top
    chosen = (flat[:, None] == jnp.arange(groups, dtype=jnp.int32)[None, :]).astype(jnp.bfloat16)
    earlier = (
        jnp.arange(count, dtype=jnp.int32)[None, :] < jnp.arange(count, dtype=jnp.int32)[:, None]
    ).astype(jnp.bfloat16)
    before = jnp.dot(earlier, chosen, preferred_element_type=jnp.float32)
    position = jnp.sum(before * chosen.astype(jnp.float32), axis=1).astype(jnp.int32)
    position = position.reshape(rows, top)
    group_hit = ids.T[:, None, None, :] == jnp.arange(groups, dtype=jnp.int32)[None, :, None, None]
    slot_hit = position.T[:, None, None, :] == jnp.arange(slots, dtype=jnp.int32)[None, None, :, None]
    return (group_hit & slot_hit).astype(jnp.bfloat16)


def body(tokens, routes, combine, up_weight, down_weight):
    rows = tokens.shape[0]
    top = routes.shape[2]
    groups = lax.axis_size("expert")
    slots = min(rows, rows * top * 9 // (8 * groups))
    slots = -(-slots // 8) * 8
    up_local = up_weight.reshape(up_weight.shape[2], up_weight.shape[3])
    down_local = down_weight.reshape(down_weight.shape[2], down_weight.shape[3])
    partner_up, partner_down = swapped((up_local, down_local), "section", 0)
    state = tokens
    for tick in range(TICKS):
        if tick > 0:
            state = shifted(state, "section", 2)
        weights = combine[tick]
        select = slot_tables(routes[tick], groups, slots)
        state_f = state.astype(jnp.float32)
        normed = (
            state_f * lax.rsqrt(jnp.mean(state_f * state_f, axis=1, keepdims=True) + 1e-06)
        ).astype(jnp.bfloat16)
        share = weights / jnp.sum(weights, axis=1, keepdims=True)
        dispatch = jnp.sum(select, axis=0)
        outgoing = jnp.einsum(
            "gsr,rd->gsd", dispatch, normed, preferred_element_type=jnp.float32
        ).astype(jnp.bfloat16)
        received = lax.all_to_all(outgoing, "expert", split_axis=0, concat_axis=0, tiled=True)
        expert_out = expert_full(
            received.reshape(groups * slots, -1), up_local, down_local, partner_up, partner_down
        ).reshape(groups, slots, -1)
        answers = lax.all_to_all(expert_out, "expert", split_axis=0, concat_axis=0, tiled=True)
        total = state_f
        for k in range(top):
            picked = jnp.einsum(
                "gsr,gsd->rd", select[k], answers, preferred_element_type=jnp.float32
            )
            total = total + share[:, k : k + 1] * picked
        state = total.astype(jnp.bfloat16)
    return state


def solution(mesh):
    in_specs = (
        P(("section", "expert"), None),
        P(None, ("section", "expert"), None),
        P(None, ("section", "expert"), None),
        P("section", "expert", None, None),
        P("section", "expert", None, None),
    )
    out_specs = P(("section", "expert"), None)
    return jax.shard_map(body, mesh=mesh, in_specs=in_specs, out_specs=out_specs, check_vma=False)
```
